512 devices in a mesh: pix: 128 (over y, x, z_hi, core), frm: 4 (over z_lo).
Axes of the slice: x: 4, y: 8, z: 8 (z_hi: 2, z_lo: 4; z = z_hi * 4 + z_lo), core: 2. Of those that a mesh axis runs over, the one named last changes fastest.
Arguments:
- video: bfloat16 [245760, 4096], P('pix', 'frm'), may hold values from -6 to 6
- shapes: bfloat16 [245760, 128], P('pix'), may hold values from -1.25 to 1.25
- valid: int32 [245760], P('pix'), may hold values 0 or 1
- omega: float32 [128], replicated, may hold values from 250 to 9000
- damping: float32 [128], replicated, may hold values from 0.3 to 30
- phase: float32 [128], replicated, may hold values from -3.140625 to 3.140625
Outputs:
- shape_grad: bfloat16 [245760, 128], P('pix')
- omega_grad: float32 [128], replicated
- damping_grad: float32 [128], replicated
- phase_grad: float32 [128], replicated
The draws below stay inside these ranges and needn't reach their ends.
All inputs are finite; a program needn't handle non-finite values. No bound on the sum of `valid` on one device may be relied on, other than what follows from the above.
Results may differ from the reference program's by a relative error of at most 0.012.
Values may be sent and summed in bfloat16 or wider, within the bound.
No kernel may reach another device: no remote copies, remote signals or barrier semaphores. Data moves between devices by JAX's collectives and lax.ppermute only.
A program may use at most 64 MiB of HBM per device.

```python
import math
import jax
import jax.numpy as jnp
from jax import lax

K = 128
FRAMES = 4096
IMG_W = 128
P_DEV = 1920
ROWS = 1920
PIXELS = 245760
N_PIX = 128


def touch_ends(array, key, least, top_value):
    place = [jax.random.randint(jax.random.fold_in(key, axis), (), 0, length) for axis, length in enumerate(array.shape)]
    main_axis = array.shape.index(max(array.shape))
    beside = place[:main_axis] + [(place[main_axis] + 1) % array.shape[main_axis]] + place[main_axis + 1:]
    return array.at[tuple(place)].set(least).at[tuple(beside)].set(top_value)


def steps_of(stream_key, extent, pieces, least, top_value):
    def one(position, parts):
        heights = jax.random.uniform(jax.random.fold_in(jax.random.fold_in(stream_key, 6), position), (parts,), jnp.float32, least / len(pieces), top_value / len(pieces))
        return jnp.repeat(jnp.exp(heights), extent[position] // parts).reshape((-1,) + (1,) * (len(extent) - position - 1))

    loudness = one(*pieces[0])
    for cut in pieces[1:]:
        loudness = loudness * one(*cut)
    return loudness


def normal_values(rng, dims, width, reach, cuts=(), kind=jnp.bfloat16):
    level = steps_of(rng, dims, cuts, -0.22, 0.18) if cuts else 1.0
    values = jax.random.normal(rng, dims, jnp.float32) * width * level
    return jnp.minimum(jnp.maximum(values, -reach), reach).astype(kind)


def setup_inputs(seed: int = 0) -> dict:
    keys = jax.random.split(jax.random.key(seed), 7)
    video = normal_values(keys[0], (PIXELS, FRAMES), 1.0, 6.0, ((0, 128), (1, 4)))
    shapes = normal_values(keys[1], (PIXELS, K), (K ** -0.5), 1.25, ((0, 128),))
    valid = touch_ends((jax.random.randint(keys[2], (PIXELS,), 0, 8) < 7).astype(jnp.int32), jax.random.fold_in(keys[2], 1), 0, 1)
    omega = jnp.clip(jnp.exp(jax.random.uniform(keys[3], (K,), jnp.float32, math.log(250.0), math.log(9000.0))), 250.0, 9000.0)
    damping = jnp.clip(jnp.exp(jax.random.uniform(keys[4], (K,), jnp.float32, math.log(0.3), math.log(30.0))), 0.3, 30.0)
    phase = jnp.clip(jax.random.uniform(keys[5], (K,), jnp.float32, -3.140625, 3.140625), -3.140625, 3.140625)
    return dict(video=video, shapes=shapes, valid=valid, omega=omega, damping=damping, phase=phase)


def modal_basis(omega, damping, phase):
    times = jnp.arange(FRAMES).astype(jnp.float32) / FRAMES
    envelope = jnp.exp(-damping[:, None] * times[None, :])
    angle_all = omega[:, None] * times[None, :] + phase[:, None]
    return envelope * jnp.cos(angle_all), envelope * jnp.sin(angle_all), times


def reference(video, shapes, valid, omega, damping, phase):
    scale = FRAMES ** -0.5
    cosine, sine, times = modal_basis(omega, damping, phase)
    basis = cosine.astype(jnp.bfloat16)
    video_blocks = video.reshape(N_PIX, P_DEV, FRAMES)
    shape_blocks = shapes.reshape(N_PIX, P_DEV, K)
    valid_blocks = valid.reshape(N_PIX, P_DEV)

    def block_step(total, items):
        frames_block, shape_block, valid_block = items
        model = jnp.dot(shape_block, basis, preferred_element_type=jnp.float32)
        resid = (valid_block[:, None].astype(jnp.float32) * (model - frames_block.astype(jnp.float32))).astype(jnp.bfloat16)
        data_grad = scale * lax.dot_general(resid, basis, (((1,), (1,)), ((), ())), preferred_element_type=jnp.float32)
        part = scale * lax.dot_general(shape_block, resid, (((0,), (0,)), ((), ())), preferred_element_type=jnp.float32)
        return total + part, data_grad

    mode_basis_grad, data_grads = lax.scan(block_step, jnp.zeros((K, FRAMES), jnp.float32), (video_blocks, shape_blocks, valid_blocks))
    grid = shapes.astype(jnp.float32).reshape(ROWS, IMG_W, K)
    padded = jnp.pad(grid, ((1, 1), (0, 0), (0, 0)))
    rows_at = jnp.arange(ROWS)
    count = ((rows_at > 0).astype(jnp.float32) + (rows_at < ROWS - 1).astype(jnp.float32))[:, None, None]
    smooth = 4.0 * (count * grid - padded[:-2] - padded[2:])
    shape_grad = (data_grads.reshape(PIXELS, K) + smooth.reshape(PIXELS, K)).astype(jnp.bfloat16)
    omega_grad = jnp.sum(mode_basis_grad * (-times[None, :] * sine), axis=1)
    damping_grad = jnp.sum(mode_basis_grad * (-times[None, :] * cosine), axis=1)
    phase_grad = jnp.sum(mode_basis_grad * (-sine), axis=1)
    return shape_grad, omega_grad, damping_grad, phase_grad
```

```python
import jax
import jax.numpy as jnp
from jax import lax
from jax.sharding import PartitionSpec as P

FRAMES = 4096
IMG_W = 128


def with_halo(cells, sides, width):
    for axis, dim in sides:
        count = lax.axis_size(axis)
        ends = count - 1
        head = lax.slice_in_dim(cells, 0, width, axis=dim)
        tail = lax.slice_in_dim(cells, cells.shape[dim] - width, cells.shape[dim], axis=dim)
        cells = jnp.concatenate(
            [
                lax.ppermute(tail, axis, [(i, (i + 1) % count) for i in range(ends)]),
                cells,
                lax.ppermute(head, axis, [((i + 1) % count, i) for i in range(ends)]),
            ],
            axis=dim,
        )
    return cells


def mode_terms(basis_grad, cosine, sine, times):
    omega_part = jnp.sum(basis_grad * (-times[None, :] * sine), axis=1)
    damping_part = jnp.sum(basis_grad * (-times[None, :] * cosine), axis=1)
    phase_part = jnp.sum(basis_grad * -sine, axis=1)
    return jnp.stack([omega_part, damping_part, phase_part])


def butterfly(x, axis):
    count = lax.axis_size(axis)
    bit = 1
    while bit < count:
        x = x + lax.ppermute(x, axis, [(i, i ^ bit) for i in range(count)])
        bit *= 2
    return x


def split_f32(x):
    top = lax.reduce_precision(x, exponent_bits=8, mantissa_bits=7)
    return top.astype(jnp.bfloat16), (x - top).astype(jnp.bfloat16)


def body(video, shapes, valid, omega, damping, phase):
    frames_local = video.shape[1]
    scale = FRAMES ** (-0.5)
    n_frm = lax.axis_size("frm")
    me = lax.axis_index("frm")
    first = me * frames_local
    times = (first + jnp.arange(frames_local)).astype(jnp.float32) / FRAMES
    envelope = jnp.exp(-damping[:, None] * times[None, :])
    angle_all = omega[:, None] * times[None, :] + phase[:, None]
    cosine = envelope * jnp.cos(angle_all)
    sine = envelope * jnp.sin(angle_all)
    basis = cosine.astype(jnp.bfloat16)

    rows_local = shapes.shape[0] // IMG_W
    grid = shapes.reshape(rows_local, IMG_W, shapes.shape[1])
    padded = with_halo(grid, (("pix", 0),), 1).astype(jnp.float32)

    model = jnp.dot(shapes, basis, preferred_element_type=jnp.float32)
    resid = (valid[:, None].astype(jnp.float32) * (model - video.astype(jnp.float32))).astype(
        jnp.bfloat16
    )
    basis_part = scale * lax.dot_general(
        shapes, resid, (((0,), (0,)), ((), ())), preferred_element_type=jnp.float32
    )
    terms = butterfly(mode_terms(basis_part, cosine, sine, times), "pix")

    data_part = scale * lax.dot_general(
        resid, basis, (((1,), (1,)), ((), ())), preferred_element_type=jnp.float32
    )
    n_pixels, n_modes = data_part.shape
    quarter = n_pixels // n_frm
    parts = data_part.reshape(n_frm, quarter, n_modes)
    acc = jnp.take(parts, me, axis=0)
    for s in range(1, n_frm):
        send = jnp.take(parts, (me + s) % n_frm, axis=0)
        acc = acc + lax.ppermute(send, "frm", [(i, (i + s) % n_frm) for i in range(n_frm)])

    rows_total = rows_local * lax.axis_size("pix")
    rows_at = lax.axis_index("pix") * rows_local + jnp.arange(rows_local)
    count = ((rows_at > 0).astype(jnp.float32) + (rows_at < rows_total - 1).astype(jnp.float32))[
        :, None, None
    ]
    smooth = 4.0 * (count * grid.astype(jnp.float32) - padded[:-2] - padded[2:])
    smooth_parts = smooth.reshape(n_frm, quarter, n_modes)
    own = (acc + jnp.take(smooth_parts, me, axis=0)).astype(jnp.bfloat16)

    hi, lo = split_f32(terms)
    extra = 16 - (quarter + 2 * terms.shape[0]) % 16
    packet = jnp.concatenate(
        [own, hi, lo, jnp.zeros((extra % 16, n_modes), jnp.bfloat16)], axis=0
    )
    got = [packet]
    for s in range(1, n_frm):
        got.append(lax.ppermute(packet, "frm", [(i, (i + s) % n_frm) for i in range(n_frm)]))
    stacked = jnp.stack(got)
    ordered = jnp.take(stacked, (me - jnp.arange(n_frm)) % n_frm, axis=0)
    shape_grad = ordered[:, :quarter].reshape(n_pixels, n_modes)
    k = terms.shape[0]
    hi_all = ordered[:, quarter : quarter + k].astype(jnp.float32)
    lo_all = ordered[:, quarter + k : quarter + 2 * k].astype(jnp.float32)
    pieces = hi_all + lo_all
    total = pieces[0]
    for f in range(1, n_frm):
        total = total + pieces[f]
    return (shape_grad, total[0], total[1], total[2])


def solution(mesh):
    placed = (P("pix", "frm"), P("pix", None), P("pix"), P(), P(), P())
    return jax.shard_map(
        body, mesh=mesh, in_specs=placed, out_specs=(P("pix", None), P(), P(), P()), check_vma=False
    )
```

```python
import jax
import jax.numpy as jnp
from jax import lax
from jax.experimental import pallas as pl
from jax.experimental.pallas import tpu as pltpu
from jax.sharding import PartitionSpec as P

FRAMES = 4096
IMG_W = 128


def with_halo(cells, sides, width):
    for axis, dim in sides:
        count = lax.axis_size(axis)
        ends = count - 1
        head = lax.slice_in_dim(cells, 0, width, axis=dim)
        tail = lax.slice_in_dim(cells, cells.shape[dim] - width, cells.shape[dim], axis=dim)
        cells = jnp.concatenate(
            [
                lax.ppermute(tail, axis, [(i, (i + 1) % count) for i in range(ends)]),
                cells,
                lax.ppermute(head, axis, [((i + 1) % count, i) for i in range(ends)]),
            ],
            axis=dim,
        )
    return cells


def mode_terms(basis_grad, cosine, sine, times):
    omega_part = jnp.sum(basis_grad * (-times[None, :] * sine), axis=1)
    damping_part = jnp.sum(basis_grad * (-times[None, :] * cosine), axis=1)
    phase_part = jnp.sum(basis_grad * -sine, axis=1)
    return jnp.stack([omega_part, damping_part, phase_part])


def butterfly(x, axis):
    count = lax.axis_size(axis)
    bit = 1
    while bit < count:
        x = x + lax.ppermute(x, axis, [(i, i ^ bit) for i in range(count)])
        bit *= 2
    return x


def fit_kernel(shapes_ref, shapes_t_ref, video_ref, valid_ref, basis_ref, basis_t_ref, data_ref, mode_ref):
    step = pl.program_id(0)
    model = jnp.dot(shapes_ref[...], basis_ref[...], preferred_element_type=jnp.float32)
    resid = (valid_ref[...] * (model - video_ref[...].astype(jnp.float32))).astype(jnp.bfloat16)
    data_ref[...] = jnp.dot(resid, basis_t_ref[...], preferred_element_type=jnp.float32)
    part = jnp.dot(shapes_t_ref[...], resid, preferred_element_type=jnp.float32)

    @pl.when(step == 0)
    def _():
        mode_ref[...] = part

    @pl.when(step > 0)
    def _():
        mode_ref[...] += part


def fit(shapes, video, valid, basis, tile=384):
    n_pixels, n_modes = shapes.shape
    n_frames = video.shape[1]
    flops = 3 * 2 * n_pixels * n_modes * n_frames
    moved = video.size * 2 + shapes.size * 4 + n_pixels * n_modes * 4 + n_modes * n_frames * 8
    return pl.pallas_call(
        fit_kernel,
        grid=(n_pixels // tile,),
        in_specs=[
            pl.BlockSpec((tile, n_modes), lambda i: (i, 0)),
            pl.BlockSpec((n_modes, tile), lambda i: (0, i)),
            pl.BlockSpec((tile, n_frames), lambda i: (i, 0)),
            pl.BlockSpec((tile, 1), lambda i: (i, 0)),
            pl.BlockSpec((n_modes, n_frames), lambda i: (0, 0)),
            pl.BlockSpec((n_frames, n_modes), lambda i: (0, 0)),
        ],
        out_specs=[
            pl.BlockSpec((tile, n_modes), lambda i: (i, 0)),
            pl.BlockSpec((n_modes, n_frames), lambda i: (0, 0)),
        ],
        out_shape=[
            jax.ShapeDtypeStruct((n_pixels, n_modes), jnp.float32),
            jax.ShapeDtypeStruct((n_modes, n_frames), jnp.float32),
        ],
        compiler_params=pltpu.CompilerParams(dimension_semantics=("arbitrary",)),
        cost_estimate=pl.CostEstimate(flops=flops, bytes_accessed=moved, transcendentals=0),
    )(shapes, shapes.T, video, valid.astype(jnp.float32)[:, None], basis, basis.T)


def body(video, shapes, valid, omega, damping, phase):
    frames_local = video.shape[1]
    scale = FRAMES ** (-0.5)
    n_frm = lax.axis_size("frm")
    me = lax.axis_index("frm")
    first = me * frames_local
    times = (first + jnp.arange(frames_local)).astype(jnp.float32) / FRAMES
    envelope = jnp.exp(-damping[:, None] * times[None, :])
    angle_all = omega[:, None] * times[None, :] + phase[:, None]
    cosine = envelope * jnp.cos(angle_all)
    sine = envelope * jnp.sin(angle_all)
    basis = cosine.astype(jnp.bfloat16)

    rows_local = shapes.shape[0] // IMG_W
    grid = shapes.reshape(rows_local, IMG_W, shapes.shape[1])
    padded = with_halo(grid, (("pix", 0),), 1).astype(jnp.float32)

    data_raw, mode_raw = fit(shapes, video, valid, basis)
    terms = butterfly(butterfly(mode_terms(scale * mode_raw, cosine, sine, times), "pix"), "frm")
    data_part = scale * data_raw
    n_pixels, n_modes = data_part.shape
    quarter = n_pixels // n_frm
    parts = data_part.reshape(n_frm, quarter, n_modes)
    acc = jnp.take(parts, me, axis=0)
    for s in range(1, n_frm):
        send = jnp.take(parts, (me + s) % n_frm, axis=0)
        acc = acc + lax.ppermute(send, "frm", [(i, (i + s) % n_frm) for i in range(n_frm)])

    rows_total = rows_local * lax.axis_size("pix")
    rows_at = lax.axis_index("pix") * rows_local + jnp.arange(rows_local)
    count = ((rows_at > 0).astype(jnp.float32) + (rows_at < rows_total - 1).astype(jnp.float32))[
        :, None, None
    ]
    smooth = 4.0 * (count * grid.astype(jnp.float32) - padded[:-2] - padded[2:])
    smooth_parts = smooth.reshape(n_frm, quarter, n_modes)
    own = (acc + jnp.take(smooth_parts, me, axis=0)).astype(jnp.bfloat16)

    packet = own
    got = [packet]
    for s in range(1, n_frm):
        got.append(lax.ppermute(packet, "frm", [(i, (i + s) % n_frm) for i in range(n_frm)]))
    stacked = jnp.stack(got)
    ordered = jnp.take(stacked, (me - jnp.arange(n_frm)) % n_frm, axis=0)
    shape_grad = ordered.reshape(n_pixels, n_modes)
    return (shape_grad, terms[0], terms[1], terms[2])


def solution(mesh):
    placed = (P("pix", "frm"), P("pix", None), P("pix"), P(), P(), P())
    return jax.shard_map(
        body, mesh=mesh, in_specs=placed, out_specs=(P("pix", None), P(), P(), P()), check_vma=False
    )
```

```python
import jax
import jax.numpy as jnp
from jax import lax
from jax.experimental import pallas as pl
from jax.experimental.pallas import tpu as pltpu
from jax.sharding import PartitionSpec as P

FRAMES = 4096
IMG_W = 128


def with_halo(cells, sides, width):
    for axis, dim in sides:
        count = lax.axis_size(axis)
        ends = count - 1
        head = lax.slice_in_dim(cells, 0, width, axis=dim)
        tail = lax.slice_in_dim(cells, cells.shape[dim] - width, cells.shape[dim], axis=dim)
        cells = jnp.concatenate(
            [
                lax.ppermute(tail, axis, [(i, (i + 1) % count) for i in range(ends)]),
                cells,
                lax.ppermute(head, axis, [((i + 1) % count, i) for i in range(ends)]),
            ],
            axis=dim,
        )
    return cells


def mode_terms(basis_grad, cosine, sine, times):
    omega_part = jnp.sum(basis_grad * (-times[None, :] * sine), axis=1)
    damping_part = jnp.sum(basis_grad * (-times[None, :] * cosine), axis=1)
    phase_part = jnp.sum(basis_grad * -sine, axis=1)
    return jnp.stack([omega_part, damping_part, phase_part])


def split_f32(x):
    top = lax.reduce_precision(x, exponent_bits=8, mantissa_bits=7)
    return top.astype(jnp.bfloat16), (x - top).astype(jnp.bfloat16)


def sum_over(x, axis):
    count = lax.axis_size(axis)
    copies = lax.all_to_all(jnp.broadcast_to(x[None], (count,) + x.shape), axis, 0, 0, tiled=False)
    return jnp.sum(copies, axis=0)


def butterfly(x, axis):
    count = lax.axis_size(axis)
    bit = 1
    while bit < count:
        x = x + lax.ppermute(x, axis, [(i, i ^ bit) for i in range(count)])
        bit *= 2
    return x


def fit_kernel(shapes_ref, shapes_t_ref, video_ref, valid_ref, basis_ref, data_ref, mode_ref):
    step = pl.program_id(0)
    model = jnp.dot(shapes_ref[...], basis_ref[...], preferred_element_type=jnp.float32)
    resid = (valid_ref[...] * (model - video_ref[...].astype(jnp.float32))).astype(jnp.bfloat16)
    data_ref[...] = lax.dot_general(
        resid, basis_ref[...], (((1,), (1,)), ((), ())), preferred_element_type=jnp.float32
    )
    part = jnp.dot(shapes_t_ref[...], resid, preferred_element_type=jnp.float32)

    @pl.when(step == 0)
    def _():
        mode_ref[...] = part

    @pl.when(step > 0)
    def _():
        mode_ref[...] += part


def fit(shapes, video, valid, basis, tile=384):
    n_pixels, n_modes = shapes.shape
    n_frames = video.shape[1]
    flops = 3 * 2 * n_pixels * n_modes * n_frames
    moved = video.size * 2 + shapes.size * 4 + n_pixels * n_modes * 4 + n_modes * n_frames * 8
    return pl.pallas_call(
        fit_kernel,
        grid=(n_pixels // tile,),
        in_specs=[
            pl.BlockSpec((tile, n_modes), lambda i: (i, 0)),
            pl.BlockSpec((n_modes, tile), lambda i: (0, i)),
            pl.BlockSpec((tile, n_frames), lambda i: (i, 0)),
            pl.BlockSpec((tile, 1), lambda i: (i, 0)),
            pl.BlockSpec((n_modes, n_frames), lambda i: (0, 0)),
        ],
        out_specs=[
            pl.BlockSpec((tile, n_modes), lambda i: (i, 0)),
            pl.BlockSpec((n_modes, n_frames), lambda i: (0, 0)),
        ],
        out_shape=[
            jax.ShapeDtypeStruct((n_pixels, n_modes), jnp.float32),
            jax.ShapeDtypeStruct((n_modes, n_frames), jnp.float32),
        ],
        compiler_params=pltpu.CompilerParams(dimension_semantics=("arbitrary",)),
        cost_estimate=pl.CostEstimate(flops=flops, bytes_accessed=moved, transcendentals=0),
    )(shapes, shapes.T, video, valid.astype(jnp.float32)[:, None], basis)


def body(video, shapes, valid, omega, damping, phase):
    frames_local = video.shape[1]
    scale = FRAMES ** (-0.5)
    n_frm = lax.axis_size("frm")
    me = lax.axis_index("frm")
    first = me * frames_local
    times = (first + jnp.arange(frames_local)).astype(jnp.float32) / FRAMES
    envelope = jnp.exp(-damping[:, None] * times[None, :])
    angle_all = omega[:, None] * times[None, :] + phase[:, None]
    cosine, sine = lax.optimization_barrier(
        (envelope * jnp.cos(angle_all), envelope * jnp.sin(angle_all))
    )
    basis = cosine.astype(jnp.bfloat16)

    rows_local = shapes.shape[0] // IMG_W
    grid = shapes.reshape(rows_local, IMG_W, shapes.shape[1])
    padded = with_halo(grid, (("pix", 0),), 1).astype(jnp.float32)

    data_raw, mode_raw = fit(shapes, video, valid, basis)
    data_part = scale * data_raw
    local_terms = mode_terms(scale * mode_raw, cosine, sine, times)
    n_pixels, n_modes = data_part.shape
    quarter = n_pixels // n_frm
    parts = data_part.reshape(n_frm, quarter, n_modes)
    acc = jnp.take(parts, me, axis=0)
    for s in range(1, n_frm):
        send = jnp.take(parts, (me + s) % n_frm, axis=0)
        acc = acc + lax.ppermute(send, "frm", [(i, (i + s) % n_frm) for i in range(n_frm)])
    terms = sum_over(local_terms, "pix")

    rows_total = rows_local * lax.axis_size("pix")
    rows_at = lax.axis_index("pix") * rows_local + jnp.arange(rows_local)
    count = ((rows_at > 0).astype(jnp.float32) + (rows_at < rows_total - 1).astype(jnp.float32))[
        :, None, None
    ]
    smooth = 4.0 * (count * grid.astype(jnp.float32) - padded[:-2] - padded[2:])
    smooth_parts = smooth.reshape(n_frm, quarter, n_modes)
    own = (acc + jnp.take(smooth_parts, me, axis=0)).astype(jnp.bfloat16)

    hi, lo = split_f32(terms)
    k = terms.shape[0]
    extra = (-(quarter + 2 * k)) % 16
    packet = jnp.concatenate([own, hi, lo, jnp.zeros((extra, n_modes), jnp.bfloat16)], axis=0)
    got = [packet]
    for s in range(1, n_frm):
        got.append(lax.ppermute(packet, "frm", [(i, (i + s) % n_frm) for i in range(n_frm)]))
    stacked = jnp.stack(got)
    ordered = jnp.take(stacked, (me - jnp.arange(n_frm)) % n_frm, axis=0)
    shape_grad = ordered[:, :quarter].reshape(n_pixels, n_modes)
    pieces = ordered[:, quarter : quarter + k].astype(jnp.float32) + ordered[
        :, quarter + k : quarter + 2 * k
    ].astype(jnp.float32)
    total = pieces[0]
    for f in range(1, n_frm):
        total = total + pieces[f]
    return (shape_grad, total[0], total[1], total[2])


def solution(mesh):
    placed = (P("pix", "frm"), P("pix", None), P("pix"), P(), P(), P())
    return jax.shard_map(
        body, mesh=mesh, in_specs=placed, out_specs=(P("pix", None), P(), P(), P()), check_vma=False
    )
```

```python
import jax
import jax.numpy as jnp
from jax import lax
from jax.experimental import pallas as pl
from jax.experimental.pallas import tpu as pltpu
from jax.sharding import PartitionSpec as P


FRAMES = 4096
IMG_W = 128


def with_halo(cells, sides, width):
    for axis, dim in sides:
        count = lax.axis_size(axis)
        ends = count - 1
        head = lax.slice_in_dim(cells, 0, width, axis=dim)
        tail = lax.slice_in_dim(cells, cells.shape[dim] - width, cells.shape[dim], axis=dim)
        cells = jnp.concatenate(
            [
                lax.ppermute(tail, axis, [(i, (i + 1) % count) for i in range(ends)]),
                cells,
                lax.ppermute(head, axis, [((i + 1) % count, i) for i in range(ends)]),
            ],
            axis=dim,
        )
    return cells


def mode_terms(basis_grad, cosine, sine, times):
    omega_part = jnp.sum(basis_grad * (-times[None, :] * sine), axis=1)
    damping_part = jnp.sum(basis_grad * (-times[None, :] * cosine), axis=1)
    phase_part = jnp.sum(basis_grad * -sine, axis=1)
    return jnp.stack([omega_part, damping_part, phase_part])


def split_f32(x):
    top = lax.reduce_precision(x, exponent_bits=8, mantissa_bits=7)
    return top.astype(jnp.bfloat16), (x - top).astype(jnp.bfloat16)


def sum_over(x, axis):
    count = lax.axis_size(axis)
    copies = lax.all_to_all(jnp.broadcast_to(x[None], (count,) + x.shape), axis, 0, 0, tiled=False)
    return jnp.sum(copies, axis=0)


def fit_kernel(shapes_ref, shapes_t_ref, video_ref, valid_ref, basis_ref, data_ref, mode_ref):
    step = pl.program_id(0)
    model = jnp.dot(shapes_ref[...], basis_ref[...], preferred_element_type=jnp.float32)
    resid = (valid_ref[...] * (model - video_ref[...].astype(jnp.float32))).astype(jnp.bfloat16)
    data_ref[...] = lax.dot_general(
        resid, basis_ref[...], (((1,), (1,)), ((), ())), preferred_element_type=jnp.float32
    )
    part = jnp.dot(shapes_t_ref[...], resid, preferred_element_type=jnp.float32)

    @pl.when(step == 0)
    def _():
        mode_ref[...] = part

    @pl.when(step > 0)
    def _():
        mode_ref[...] += part


def fit(shapes, video, valid, basis, tile=384):
    n_pixels, n_modes = shapes.shape
    n_frames = video.shape[1]
    flops = 3 * 2 * n_pixels * n_modes * n_frames
    moved = video.size * 2 + shapes.size * 4 + n_pixels * n_modes * 4 + n_modes * n_frames * 8
    return pl.pallas_call(
        fit_kernel,
        grid=(n_pixels // tile,),
        in_specs=[
            pl.BlockSpec((tile, n_modes), lambda i: (i, 0)),
            pl.BlockSpec((n_modes, tile), lambda i: (0, i)),
            pl.BlockSpec((tile, n_frames), lambda i: (i, 0)),
            pl.BlockSpec((tile, 1), lambda i: (i, 0)),
            pl.BlockSpec((n_modes, n_frames), lambda i: (0, 0)),
        ],
        out_specs=[
            pl.BlockSpec((tile, n_modes), lambda i: (i, 0)),
            pl.BlockSpec((n_modes, n_frames), lambda i: (0, 0)),
        ],
        out_shape=[
            jax.ShapeDtypeStruct((n_pixels, n_modes), jnp.float32),
            jax.ShapeDtypeStruct((n_modes, n_frames), jnp.float32),
        ],
        compiler_params=pltpu.CompilerParams(dimension_semantics=("arbitrary",)),
        cost_estimate=pl.CostEstimate(flops=flops, bytes_accessed=moved, transcendentals=0),
    )(shapes, shapes.T, video, valid.astype(jnp.float32)[:, None], basis)


def body(video, shapes, valid, omega, damping, phase):
    frames_local = video.shape[1]
    scale = FRAMES ** (-0.5)
    n_frm = lax.axis_size("frm")
    me = lax.axis_index("frm")
    first = me * frames_local
    times = (first + jnp.arange(frames_local)).astype(jnp.float32) / FRAMES
    envelope = jnp.exp(-damping[:, None] * times[None, :])
    angle_all = omega[:, None] * times[None, :] + phase[:, None]
    cosine, sine = lax.optimization_barrier(
        (envelope * jnp.cos(angle_all), envelope * jnp.sin(angle_all))
    )
    basis = cosine.astype(jnp.bfloat16)

    rows_local = shapes.shape[0] // IMG_W
    grid = shapes.reshape(rows_local, IMG_W, shapes.shape[1])
    padded = with_halo(grid, (("pix", 0),), 1).astype(jnp.float32)

    data_raw, mode_raw = fit(shapes, video, valid, basis)
    data_part = scale * data_raw
    local_terms = mode_terms(scale * mode_raw, cosine, sine, times)
    n_pixels, n_modes = data_part.shape
    quarter = n_pixels // n_frm
    parts = data_part.reshape(n_frm, quarter, n_modes)
    acc = jnp.take(parts, me, axis=0)
    for s in range(1, n_frm):
        send = jnp.take(parts, (me + s) % n_frm, axis=0)
        acc = acc + lax.ppermute(send, "frm", [(i, (i + s) % n_frm) for i in range(n_frm)])
    terms = sum_over(local_terms, "pix")

    rows_total = rows_local * lax.axis_size("pix")
    rows_at = lax.axis_index("pix") * rows_local + jnp.arange(rows_local)
    count = ((rows_at > 0).astype(jnp.float32) + (rows_at < rows_total - 1).astype(jnp.float32))[
        :, None, None
    ]
    smooth = 4.0 * (count * grid.astype(jnp.float32) - padded[:-2] - padded[2:])
    smooth_parts = smooth.reshape(n_frm, quarter, n_modes)
    own = (acc + jnp.take(smooth_parts, me, axis=0)).astype(jnp.bfloat16)

    hi, lo = split_f32(terms)
    k = terms.shape[0]
    extra = (-(quarter + 2 * k)) % 16
    packet = jnp.concatenate([own, hi, lo, jnp.zeros((extra, n_modes), jnp.bfloat16)], axis=0)
    got = [packet]
    for s in range(1, n_frm):
        got.append(lax.ppermute(packet, "frm", [(i, (i + s) % n_frm) for i in range(n_frm)]))
    stacked = jnp.stack(got)
    ordered = jnp.take(stacked, (me - jnp.arange(n_frm)) % n_frm, axis=0)
    shape_grad = ordered[:, :quarter].reshape(n_pixels, n_modes)
    pieces = ordered[:, quarter : quarter + k].astype(jnp.float32) + ordered[
        :, quarter + k : quarter + 2 * k
    ].astype(jnp.float32)
    total = pieces[0]
    for f in range(1, n_frm):
        total = total + pieces[f]
    return (shape_grad, total[0], total[1], total[2])


def solution(mesh):
    placed = (P("pix", "frm"), P("pix", None), P("pix"), P(), P(), P())
    return jax.shard_map(
        body,
        mesh=mesh,
        in_specs=placed,
        out_specs=(P("pix", None), P(), P(), P()),
        check_vma=False,
    )
```

```python
import jax
import jax.numpy as jnp
from jax import lax
from jax.experimental import pallas as pl
from jax.experimental.pallas import tpu as pltpu
from jax.sharding import PartitionSpec as P

FRAMES = 4096
IMG_W = 128


def with_halo(cells, sides, width):
    for axis, dim in sides:
        count = lax.axis_size(axis)
        ends = count - 1
        head = lax.slice_in_dim(cells, 0, width, axis=dim)
        tail = lax.slice_in_dim(cells, cells.shape[dim] - width, cells.shape[dim], axis=dim)
        cells = jnp.concatenate(
            [
                lax.ppermute(tail, axis, [(i, (i + 1) % count) for i in range(ends)]),
                cells,
                lax.ppermute(head, axis, [((i + 1) % count, i) for i in range(ends)]),
            ],
            axis=dim,
        )
    return cells


def mode_terms(basis_grad, cosine, sine, times):
    omega_part = jnp.sum(basis_grad * (-times[None, :] * sine), axis=1)
    damping_part = jnp.sum(basis_grad * (-times[None, :] * cosine), axis=1)
    phase_part = jnp.sum(basis_grad * -sine, axis=1)
    return jnp.stack([omega_part, damping_part, phase_part])


def split_f32(x):
    top = lax.reduce_precision(x, exponent_bits=8, mantissa_bits=7)
    return top.astype(jnp.bfloat16), (x - top).astype(jnp.bfloat16)


def sum_over(x, axis):
    count = lax.axis_size(axis)
    copies = lax.all_to_all(jnp.broadcast_to(x[None], (count,) + x.shape), axis, 0, 0, tiled=False)
    return jnp.sum(copies, axis=0)


def butterfly(x, axis):
    count = lax.axis_size(axis)
    bit = 1
    while bit < count:
        x = x + lax.ppermute(x, axis, [(i, i ^ bit) for i in range(count)])
        bit *= 2
    return x


def fit_kernel(shapes_ref, shapes_t_ref, video_ref, basis_ref, data_ref, mode_ref):
    step = pl.program_id(0)
    model = jnp.dot(shapes_ref[...], basis_ref[...], preferred_element_type=jnp.float32)
    resid = (model - video_ref[...].astype(jnp.float32)).astype(jnp.bfloat16)
    data_ref[...] = lax.dot_general(
        resid, basis_ref[...], (((1,), (1,)), ((), ())), preferred_element_type=jnp.float32
    )
    part = jnp.dot(shapes_t_ref[...], resid, preferred_element_type=jnp.float32)

    @pl.when(step == 0)
    def _():
        mode_ref[...] = part

    @pl.when(step > 0)
    def _():
        mode_ref[...] += part


def fit(shapes, video, valid, basis, tile=640):
    n_pixels, n_modes = shapes.shape
    n_frames = video.shape[1]
    flops = 3 * 2 * n_pixels * n_modes * n_frames
    moved = video.size * 2 + shapes.size * 4 + n_pixels * n_modes * 4 + n_modes * n_frames * 8
    return pl.pallas_call(
        fit_kernel,
        grid=(n_pixels // tile,),
        in_specs=[
            pl.BlockSpec((tile, n_modes), lambda i: (i, 0)),
            pl.BlockSpec((n_modes, tile), lambda i: (0, i)),
            pl.BlockSpec((tile, n_frames), lambda i: (i, 0)),
            pl.BlockSpec((n_modes, n_frames), lambda i: (0, 0)),
        ],
        out_specs=[
            pl.BlockSpec((tile, n_modes), lambda i: (i, 0)),
            pl.BlockSpec((n_modes, n_frames), lambda i: (0, 0)),
        ],
        out_shape=[
            jax.ShapeDtypeStruct((n_pixels, n_modes), jnp.float32),
            jax.ShapeDtypeStruct((n_modes, n_frames), jnp.float32),
        ],
        compiler_params=pltpu.CompilerParams(dimension_semantics=("arbitrary",)),
        cost_estimate=pl.CostEstimate(flops=flops, bytes_accessed=moved, transcendentals=0),
    )(shapes, (shapes * valid[:, None].astype(shapes.dtype)).T, video, basis)


def body(video, shapes, valid, omega, damping, phase):
    frames_local = video.shape[1]
    scale = FRAMES ** (-0.5)
    n_frm = lax.axis_size("frm")
    me = lax.axis_index("frm")
    first = me * frames_local
    times = (first + jnp.arange(frames_local)).astype(jnp.float32) / FRAMES
    envelope = jnp.exp(-damping[:, None] * times[None, :])
    angle_all = omega[:, None] * times[None, :] + phase[:, None]
    cosine, sine = lax.optimization_barrier(
        (envelope * jnp.cos(angle_all), envelope * jnp.sin(angle_all))
    )
    basis = cosine.astype(jnp.bfloat16)

    rows_local = shapes.shape[0] // IMG_W
    grid = shapes.reshape(rows_local, IMG_W, shapes.shape[1])
    padded = with_halo(grid, (("pix", 0),), 1).astype(jnp.float32)

    data_raw, mode_raw = fit(shapes, video, valid, basis)
    data_part = scale * data_raw * valid[:, None].astype(jnp.float32)
    local_terms = mode_terms(scale * mode_raw, cosine, sine, times)
    n_pixels, n_modes = data_part.shape
    quarter = n_pixels // n_frm
    parts = data_part.reshape(n_frm, quarter, n_modes)
    acc = jnp.take(parts, me, axis=0)
    for s in range(1, n_frm):
        send = jnp.take(parts, (me + s) % n_frm, axis=0)
        acc = acc + lax.ppermute(send, "frm", [(i, (i + s) % n_frm) for i in range(n_frm)])
    terms = sum_over(local_terms, "pix")

    rows_total = rows_local * lax.axis_size("pix")
    rows_at = lax.axis_index("pix") * rows_local + jnp.arange(rows_local)
    count = ((rows_at > 0).astype(jnp.float32) + (rows_at < rows_total - 1).astype(jnp.float32))[
        :, None, None
    ]
    smooth = 4.0 * (count * grid.astype(jnp.float32) - padded[:-2] - padded[2:])
    smooth_parts = smooth.reshape(n_frm, quarter, n_modes)
    own = (acc + jnp.take(smooth_parts, me, axis=0)).astype(jnp.bfloat16)

    hi, lo = split_f32(terms)
    k = terms.shape[0]
    extra = (-(quarter + 2 * k)) % 16
    packet = jnp.concatenate([own, hi, lo, jnp.zeros((extra, n_modes), jnp.bfloat16)], axis=0)
    got = [packet]
    for s in range(1, n_frm):
        got.append(lax.ppermute(packet, "frm", [(i, (i + s) % n_frm) for i in range(n_frm)]))
    stacked = jnp.stack(got)
    ordered = jnp.take(stacked, (me - jnp.arange(n_frm)) % n_frm, axis=0)
    shape_grad = ordered[:, :quarter].reshape(n_pixels, n_modes)
    pieces = ordered[:, quarter : quarter + k].astype(jnp.float32) + ordered[
        :, quarter + k : quarter + 2 * k
    ].astype(jnp.float32)
    total = pieces[0]
    for f in range(1, n_frm):
        total = total + pieces[f]
    return (shape_grad, total[0], total[1], total[2])


def solution(mesh):
    placed = (P("pix", "frm"), P("pix", None), P("pix"), P(), P(), P())
    return jax.shard_map(
        body, mesh=mesh, in_specs=placed, out_specs=(P("pix", None), P(), P(), P()), check_vma=False
    )
```

```python
import jax
import jax.numpy as jnp
from jax import lax
from jax.experimental import pallas as pl
from jax.experimental.pallas import tpu as pltpu
from jax.sharding import PartitionSpec as P

FRAMES = 4096
IMG_W = 128


def with_halo(cells, sides, width):
    for axis, dim in sides:
        count = lax.axis_size(axis)
        ends = count - 1
        head = lax.slice_in_dim(cells, 0, width, axis=dim)
        tail = lax.slice_in_dim(cells, cells.shape[dim] - width, cells.shape[dim], axis=dim)
        cells = jnp.concatenate(
            [
                lax.ppermute(tail, axis, [(i, (i + 1) % count) for i in range(ends)]),
                cells,
                lax.ppermute(head, axis, [((i + 1) % count, i) for i in range(ends)]),
            ],
            axis=dim,
        )
    return cells


def mode_terms(basis_grad, cosine, sine, times):
    omega_part = jnp.sum(basis_grad * (-times[None, :] * sine), axis=1)
    damping_part = jnp.sum(basis_grad * (-times[None, :] * cosine), axis=1)
    phase_part = jnp.sum(basis_grad * -sine, axis=1)
    return jnp.stack([omega_part, damping_part, phase_part])


def split_f32(x):
    top = lax.reduce_precision(x, exponent_bits=8, mantissa_bits=7)
    return top.astype(jnp.bfloat16), (x - top).astype(jnp.bfloat16)


def sum_over(x, axis):
    count = lax.axis_size(axis)
    copies = lax.all_to_all(jnp.broadcast_to(x[None], (count,) + x.shape), axis, 0, 0, tiled=False)
    return jnp.sum(copies, axis=0)


def butterfly(x, axis):
    count = lax.axis_size(axis)
    bit = 1
    while bit < count:
        x = x + lax.ppermute(x, axis, [(i, i ^ bit) for i in range(count)])
        bit *= 2
    return x


def fit_kernel(shapes_ref, shapes_t_ref, video_ref, basis_ref, data_ref, mode_ref):
    step = pl.program_id(0)
    model = jnp.dot(shapes_ref[...], basis_ref[...], preferred_element_type=jnp.float32)
    resid = (model - video_ref[...].astype(jnp.float32)).astype(jnp.bfloat16)
    data_ref[...] = lax.dot_general(
        resid, basis_ref[...], (((1,), (1,)), ((), ())), preferred_element_type=jnp.float32
    )
    part = jnp.dot(shapes_t_ref[...], resid, preferred_element_type=jnp.float32)

    @pl.when(step == 0)
    def _():
        mode_ref[...] = part

    @pl.when(step > 0)
    def _():
        mode_ref[...] += part


def fit(shapes, video, valid, basis, tile=640):
    n_pixels, n_modes = shapes.shape
    n_frames = video.shape[1]
    flops = 3 * 2 * n_pixels * n_modes * n_frames
    moved = video.size * 2 + shapes.size * 4 + n_pixels * n_modes * 4 + n_modes * n_frames * 8
    return pl.pallas_call(
        fit_kernel,
        grid=(n_pixels // tile,),
        in_specs=[
            pl.BlockSpec((tile, n_modes), lambda i: (i, 0)),
            pl.BlockSpec((n_modes, tile), lambda i: (0, i)),
            pl.BlockSpec((tile, n_frames), lambda i: (i, 0)),
            pl.BlockSpec((n_modes, n_frames), lambda i: (0, 0)),
        ],
        out_specs=[
            pl.BlockSpec((tile, n_modes), lambda i: (i, 0)),
            pl.BlockSpec((n_modes, n_frames), lambda i: (0, 0)),
        ],
        out_shape=[
            jax.ShapeDtypeStruct((n_pixels, n_modes), jnp.float32),
            jax.ShapeDtypeStruct((n_modes, n_frames), jnp.float32),
        ],
        compiler_params=pltpu.CompilerParams(dimension_semantics=("arbitrary",)),
        cost_estimate=pl.CostEstimate(flops=flops, bytes_accessed=moved, transcendentals=0),
    )(shapes, (shapes * valid[:, None].astype(shapes.dtype)).T, video, basis)


def body(video, shapes, valid, omega, damping, phase):
    frames_local = video.shape[1]
    scale = FRAMES ** (-0.5)
    n_frm = lax.axis_size("frm")
    me = lax.axis_index("frm")
    first = me * frames_local
    times = (first + jnp.arange(frames_local)).astype(jnp.float32) / FRAMES
    envelope = jnp.exp(-damping[:, None] * times[None, :])
    angle_all = omega[:, None] * times[None, :] + phase[:, None]
    cosine, sine = lax.optimization_barrier(
        (envelope * jnp.cos(angle_all), envelope * jnp.sin(angle_all))
    )
    basis = cosine.astype(jnp.bfloat16)

    rows_local = shapes.shape[0] // IMG_W
    grid = shapes.reshape(rows_local, IMG_W, shapes.shape[1])
    padded = with_halo(grid, (("pix", 0),), 1).astype(jnp.float32)

    data_raw, mode_raw = fit(shapes, video, valid, basis)
    data_part = scale * data_raw * valid[:, None].astype(jnp.float32)
    local_terms = mode_terms(scale * mode_raw, cosine, sine, times)
    n_pixels, n_modes = data_part.shape
    quarter = n_pixels // n_frm
    parts = data_part.reshape(n_frm, quarter, n_modes)
    acc = jnp.take(parts, me, axis=0)
    for s in range(1, n_frm):
        send = jnp.take(parts, (me + s) % n_frm, axis=0).astype(jnp.bfloat16)
        got_part = lax.ppermute(send, "frm", [(i, (i + s) % n_frm) for i in range(n_frm)])
        acc = acc + got_part.astype(jnp.float32)
    terms = sum_over(local_terms, "pix")

    rows_total = rows_local * lax.axis_size("pix")
    rows_at = lax.axis_index("pix") * rows_local + jnp.arange(rows_local)
    count = ((rows_at > 0).astype(jnp.float32) + (rows_at < rows_total - 1).astype(jnp.float32))[
        :, None, None
    ]
    smooth = 4.0 * (count * grid.astype(jnp.float32) - padded[:-2] - padded[2:])
    smooth_parts = smooth.reshape(n_frm, quarter, n_modes)
    own = (acc + jnp.take(smooth_parts, me, axis=0)).astype(jnp.bfloat16)

    hi, lo = split_f32(terms)
    k = terms.shape[0]
    extra = (-(quarter + 2 * k)) % 16
    packet = jnp.concatenate([own, hi, lo, jnp.zeros((extra, n_modes), jnp.bfloat16)], axis=0)
    got = [packet]
    for s in range(1, n_frm):
        got.append(lax.ppermute(packet, "frm", [(i, (i + s) % n_frm) for i in range(n_frm)]))
    stacked = jnp.stack(got)
    ordered = jnp.take(stacked, (me - jnp.arange(n_frm)) % n_frm, axis=0)
    shape_grad = ordered[:, :quarter].reshape(n_pixels, n_modes)
    pieces = ordered[:, quarter : quarter + k].astype(jnp.float32) + ordered[
        :, quarter + k : quarter + 2 * k
    ].astype(jnp.float32)
    total = pieces[0]
    for f in range(1, n_frm):
        total = total + pieces[f]
    return (shape_grad, total[0], total[1], total[2])


def solution(mesh):
    placed = (P("pix", "frm"), P("pix", None), P("pix"), P(), P(), P())
    return jax.shard_map(
        body, mesh=mesh, in_specs=placed, out_specs=(P("pix", None), P(), P(), P()), check_vma=False
    )
```

```python
import jax
import jax.numpy as jnp
from jax import lax
from jax.experimental import pallas as pl
from jax.experimental.pallas import tpu as pltpu
from jax.sharding import PartitionSpec as P


FRAMES = 4096
IMG_W = 128


def with_halo(cells, sides, width):
    for axis, dim in sides:
        count = lax.axis_size(axis)
        ends = count - 1
        head = lax.slice_in_dim(cells, 0, width, axis=dim)
        tail = lax.slice_in_dim(cells, cells.shape[dim] - width, cells.shape[dim], axis=dim)
        cells = jnp.concatenate(
            [
                lax.ppermute(tail, axis, [(i, (i + 1) % count) for i in range(ends)]),
                cells,
                lax.ppermute(head, axis, [((i + 1) % count, i) for i in range(ends)]),
            ],
            axis=dim,
        )
    return cells


def mode_terms(basis_grad, cosine, sine, times):
    omega_part = jnp.sum(basis_grad * (-times[None, :] * sine), axis=1)
    damping_part = jnp.sum(basis_grad * (-times[None, :] * cosine), axis=1)
    phase_part = jnp.sum(basis_grad * -sine, axis=1)
    return jnp.stack([omega_part, damping_part, phase_part])


def split_f32(x):
    top = lax.reduce_precision(x, exponent_bits=8, mantissa_bits=7)
    return top.astype(jnp.bfloat16), (x - top).astype(jnp.bfloat16)


def sum_over(x, axis):
    count = lax.axis_size(axis)
    copies = lax.all_to_all(jnp.broadcast_to(x[None], (count,) + x.shape), axis, 0, 0, tiled=False)
    return jnp.sum(copies, axis=0)


def fit_kernel(shapes_ref, shapes_t_ref, video_ref, basis_ref, data_ref, mode_ref):
    step = pl.program_id(0)
    model = jnp.dot(shapes_ref[...], basis_ref[...], preferred_element_type=jnp.float32)
    resid = (model - video_ref[...].astype(jnp.float32)).astype(jnp.bfloat16)
    data_ref[...] = lax.dot_general(
        resid, basis_ref[...], (((1,), (1,)), ((), ())), preferred_element_type=jnp.float32
    )
    part = jnp.dot(shapes_t_ref[...], resid, preferred_element_type=jnp.float32)

    @pl.when(step == 0)
    def _():
        mode_ref[...] = part

    @pl.when(step > 0)
    def _():
        mode_ref[...] += part


def fit(shapes, video, valid, basis, tile=640):
    n_pixels, n_modes = shapes.shape
    n_frames = video.shape[1]
    flops = 3 * 2 * n_pixels * n_modes * n_frames
    moved = video.size * 2 + shapes.size * 4 + n_pixels * n_modes * 4 + n_modes * n_frames * 8
    return pl.pallas_call(
        fit_kernel,
        grid=(n_pixels // tile,),
        in_specs=[
            pl.BlockSpec((tile, n_modes), lambda i: (i, 0)),
            pl.BlockSpec((n_modes, tile), lambda i: (0, i)),
            pl.BlockSpec((tile, n_frames), lambda i: (i, 0)),
            pl.BlockSpec((n_modes, n_frames), lambda i: (0, 0)),
        ],
        out_specs=[
            pl.BlockSpec((tile, n_modes), lambda i: (i, 0)),
            pl.BlockSpec((n_modes, n_frames), lambda i: (0, 0)),
        ],
        out_shape=[
            jax.ShapeDtypeStruct((n_pixels, n_modes), jnp.float32),
            jax.ShapeDtypeStruct((n_modes, n_frames), jnp.float32),
        ],
        compiler_params=pltpu.CompilerParams(dimension_semantics=("arbitrary",)),
        cost_estimate=pl.CostEstimate(flops=flops, bytes_accessed=moved, transcendentals=0),
    )(shapes, (shapes * valid[:, None].astype(shapes.dtype)).T, video, basis)


def body(video, shapes, valid, omega, damping, phase):
    frames_local = video.shape[1]
    scale = FRAMES ** (-0.5)
    n_frm = lax.axis_size("frm")
    me = lax.axis_index("frm")
    first = me * frames_local
    times = (first + jnp.arange(frames_local)).astype(jnp.float32) / FRAMES
    envelope = jnp.exp(-damping[:, None] * times[None, :])
    angle_all = omega[:, None] * times[None, :] + phase[:, None]
    cosine, sine = lax.optimization_barrier(
        (envelope * jnp.cos(angle_all), envelope * jnp.sin(angle_all))
    )
    basis = cosine.astype(jnp.bfloat16)

    rows_local = shapes.shape[0] // IMG_W
    grid = shapes.reshape(rows_local, IMG_W, shapes.shape[1])
    padded = with_halo(grid, (("pix", 0),), 1).astype(jnp.float32)

    data_raw, mode_raw = fit(shapes, video, valid, basis)
    data_part = scale * data_raw * valid[:, None].astype(jnp.float32)
    local_terms = mode_terms(scale * mode_raw, cosine, sine, times)
    n_pixels, n_modes = data_part.shape
    quarter = n_pixels // n_frm
    parts = data_part.reshape(n_frm, quarter, n_modes)
    acc = jnp.take(parts, me, axis=0)
    for s in range(1, n_frm):
        send = jnp.take(parts, (me + s) % n_frm, axis=0).astype(jnp.bfloat16)
        got_part = lax.ppermute(send, "frm", [(i, (i + s) % n_frm) for i in range(n_frm)])
        acc = acc + got_part.astype(jnp.float32)
    terms = sum_over(local_terms, "pix")

    rows_total = rows_local * lax.axis_size("pix")
    rows_at = lax.axis_index("pix") * rows_local + jnp.arange(rows_local)
    count = ((rows_at > 0).astype(jnp.float32) + (rows_at < rows_total - 1).astype(jnp.float32))[
        :, None, None
    ]
    smooth = 4.0 * (count * grid.astype(jnp.float32) - padded[:-2] - padded[2:])
    smooth_parts = smooth.reshape(n_frm, quarter, n_modes)
    own = (acc + jnp.take(smooth_parts, me, axis=0)).astype(jnp.bfloat16)

    hi, lo = split_f32(terms)
    k = terms.shape[0]
    extra = (-(quarter + 2 * k)) % 16
    packet = jnp.concatenate([own, hi, lo, jnp.zeros((extra, n_modes), jnp.bfloat16)], axis=0)
    got = [packet]
    for s in range(1, n_frm):
        got.append(lax.ppermute(packet, "frm", [(i, (i + s) % n_frm) for i in range(n_frm)]))
    stacked = jnp.stack(got)
    ordered = jnp.take(stacked, (me - jnp.arange(n_frm)) % n_frm, axis=0)
    shape_grad = ordered[:, :quarter].reshape(n_pixels, n_modes)
    pieces = ordered[:, quarter : quarter + k].astype(jnp.float32) + ordered[
        :, quarter + k : quarter + 2 * k
    ].astype(jnp.float32)
    total = pieces[0]
    for f in range(1, n_frm):
        total = total + pieces[f]
    return (shape_grad, total[0], total[1], total[2])


def solution(mesh):
    placed = (P("pix", "frm"), P("pix", None), P("pix"), P(), P(), P())
    return jax.shard_map(
        body,
        mesh=mesh,
        in_specs=placed,
        out_specs=(P("pix", None), P(), P(), P()),
        check_vma=False,
    )
```

```python
import jax
import jax.numpy as jnp
from jax import lax
from jax.experimental import pallas as pl
from jax.experimental.pallas import tpu as pltpu
from jax.sharding import PartitionSpec as P

FRAMES = 4096
IMG_W = 128


def with_halo(cells, sides, width):
    for axis, dim in sides:
        count = lax.axis_size(axis)
        ends = count - 1
        head = lax.slice_in_dim(cells, 0, width, axis=dim)
        tail = lax.slice_in_dim(cells, cells.shape[dim] - width, cells.shape[dim], axis=dim)
        cells = jnp.concatenate(
            [
                lax.ppermute(tail, axis, [(i, (i + 1) % count) for i in range(ends)]),
                cells,
                lax.ppermute(head, axis, [((i + 1) % count, i) for i in range(ends)]),
            ],
            axis=dim,
        )
    return cells


def mode_terms(basis_grad, cosine, sine, times):
    omega_part = jnp.sum(basis_grad * (-times[None, :] * sine), axis=1)
    damping_part = jnp.sum(basis_grad * (-times[None, :] * cosine), axis=1)
    phase_part = jnp.sum(basis_grad * -sine, axis=1)
    return jnp.stack([omega_part, damping_part, phase_part])


def split_f32(x):
    top = lax.reduce_precision(x, exponent_bits=8, mantissa_bits=7)
    return top.astype(jnp.bfloat16), (x - top).astype(jnp.bfloat16)


def sum_over(x, axis):
    count = lax.axis_size(axis)
    copies = lax.all_to_all(jnp.broadcast_to(x[None], (count,) + x.shape), axis, 0, 0, tiled=False)
    return jnp.sum(copies, axis=0)


def butterfly(x, axis):
    count = lax.axis_size(axis)
    bit = 1
    while bit < count:
        x = x + lax.ppermute(x, axis, [(i, i ^ bit) for i in range(count)])
        bit *= 2
    return x


def fit_kernel(shapes_ref, shapes_t_ref, video_ref, basis_ref, data_ref, mode_ref):
    step = pl.program_id(0)
    model = jnp.dot(shapes_ref[...], basis_ref[...], preferred_element_type=jnp.float32)
    resid = (model - video_ref[...].astype(jnp.float32)).astype(jnp.bfloat16)
    data_ref[...] = lax.dot_general(
        resid, basis_ref[...], (((1,), (1,)), ((), ())), preferred_element_type=jnp.float32
    )
    part = jnp.dot(shapes_t_ref[...], resid, preferred_element_type=jnp.float32)

    @pl.when(step == 0)
    def _():
        mode_ref[...] = part

    @pl.when(step > 0)
    def _():
        mode_ref[...] += part


def fit(shapes, video, valid, basis, tile=640):
    n_pixels, n_modes = shapes.shape
    n_frames = video.shape[1]
    flops = 3 * 2 * n_pixels * n_modes * n_frames
    moved = video.size * 2 + shapes.size * 4 + n_pixels * n_modes * 4 + n_modes * n_frames * 8
    return pl.pallas_call(
        fit_kernel,
        grid=(n_pixels // tile,),
        in_specs=[
            pl.BlockSpec((tile, n_modes), lambda i: (i, 0)),
            pl.BlockSpec((n_modes, tile), lambda i: (0, i)),
            pl.BlockSpec((tile, n_frames), lambda i: (i, 0)),
            pl.BlockSpec((n_modes, n_frames), lambda i: (0, 0)),
        ],
        out_specs=[
            pl.BlockSpec((tile, n_modes), lambda i: (i, 0)),
            pl.BlockSpec((n_modes, n_frames), lambda i: (0, 0)),
        ],
        out_shape=[
            jax.ShapeDtypeStruct((n_pixels, n_modes), jnp.float32),
            jax.ShapeDtypeStruct((n_modes, n_frames), jnp.float32),
        ],
        compiler_params=pltpu.CompilerParams(dimension_semantics=("arbitrary",)),
        cost_estimate=pl.CostEstimate(flops=flops, bytes_accessed=moved, transcendentals=0),
    )(shapes, (shapes * valid[:, None].astype(shapes.dtype)).T, video, basis)


def body(video, shapes, valid, omega, damping, phase):
    frames_local = video.shape[1]
    scale = FRAMES ** (-0.5)
    n_frm = lax.axis_size("frm")
    me = lax.axis_index("frm")
    first = me * frames_local
    times = (first + jnp.arange(frames_local)).astype(jnp.float32) / FRAMES
    envelope = jnp.exp(-damping[:, None] * times[None, :])
    angle_all = omega[:, None] * times[None, :] + phase[:, None]
    cosine, sine = lax.optimization_barrier(
        (envelope * jnp.cos(angle_all), envelope * jnp.sin(angle_all))
    )
    basis = cosine.astype(jnp.bfloat16)

    rows_local = shapes.shape[0] // IMG_W
    grid = shapes.reshape(rows_local, IMG_W, shapes.shape[1])
    padded = with_halo(grid, (("pix", 0),), 1).astype(jnp.float32)

    data_raw, mode_raw = fit(shapes, video, valid, basis)
    data_part = scale * data_raw * valid[:, None].astype(jnp.float32)
    local_terms = mode_terms(scale * mode_raw, cosine, sine, times)
    n_pixels, n_modes = data_part.shape
    quarter = n_pixels // n_frm
    parts = data_part.reshape(n_frm, quarter, n_modes)
    arrived = lax.all_to_all(parts.astype(jnp.bfloat16), "frm", 0, 0, tiled=False).astype(jnp.float32)
    own_part = jnp.take(parts, me, axis=0)
    acc = jnp.sum(lax.dynamic_update_index_in_dim(arrived, own_part, me, 0), axis=0)
    terms = sum_over(local_terms, "pix")

    rows_total = rows_local * lax.axis_size("pix")
    rows_at = lax.axis_index("pix") * rows_local + jnp.arange(rows_local)
    count = ((rows_at > 0).astype(jnp.float32) + (rows_at < rows_total - 1).astype(jnp.float32))[
        :, None, None
    ]
    smooth = 4.0 * (count * grid.astype(jnp.float32) - padded[:-2] - padded[2:])
    smooth_parts = smooth.reshape(n_frm, quarter, n_modes)
    own = (acc + jnp.take(smooth_parts, me, axis=0)).astype(jnp.bfloat16)

    hi, lo = split_f32(terms)
    k = terms.shape[0]
    extra = (-(quarter + 2 * k)) % 16
    packet = jnp.concatenate([own, hi, lo, jnp.zeros((extra, n_modes), jnp.bfloat16)], axis=0)
    ordered = lax.all_to_all(
        jnp.broadcast_to(packet[None], (n_frm,) + packet.shape), "frm", 0, 0, tiled=False
    )
    shape_grad = ordered[:, :quarter].reshape(n_pixels, n_modes)
    pieces = ordered[:, quarter : quarter + k].astype(jnp.float32) + ordered[
        :, quarter + k : quarter + 2 * k
    ].astype(jnp.float32)
    total = pieces[0]
    for f in range(1, n_frm):
        total = total + pieces[f]
    return (shape_grad, total[0], total[1], total[2])


def solution(mesh):
    placed = (P("pix", "frm"), P("pix", None), P("pix"), P(), P(), P())
    return jax.shard_map(
        body, mesh=mesh, in_specs=placed, out_specs=(P("pix", None), P(), P(), P()), check_vma=False
    )
```

```python
import jax
import jax.numpy as jnp
from jax import lax
from jax.experimental import pallas as pl
from jax.experimental.pallas import tpu as pltpu
from jax.sharding import PartitionSpec as P

FRAMES = 4096
IMG_W = 128


def with_halo(cells, sides, width):
    for axis, dim in sides:
        count = lax.axis_size(axis)
        ends = count - 1
        head = lax.slice_in_dim(cells, 0, width, axis=dim)
        tail = lax.slice_in_dim(cells, cells.shape[dim] - width, cells.shape[dim], axis=dim)
        cells = jnp.concatenate(
            [
                lax.ppermute(tail, axis, [(i, (i + 1) % count) for i in range(ends)]),
                cells,
                lax.ppermute(head, axis, [((i + 1) % count, i) for i in range(ends)]),
            ],
            axis=dim,
        )
    return cells


def mode_terms(basis_grad, cosine, sine, times):
    omega_part = jnp.sum(basis_grad * (-times[None, :] * sine), axis=1)
    damping_part = jnp.sum(basis_grad * (-times[None, :] * cosine), axis=1)
    phase_part = jnp.sum(basis_grad * -sine, axis=1)
    return jnp.stack([omega_part, damping_part, phase_part])


def split_f32(x):
    top = lax.reduce_precision(x, exponent_bits=8, mantissa_bits=7)
    return top.astype(jnp.bfloat16), (x - top).astype(jnp.bfloat16)


def sum_over(x, axis):
    count = lax.axis_size(axis)
    copies = lax.all_to_all(jnp.broadcast_to(x[None], (count,) + x.shape), axis, 0, 0, tiled=False)
    return jnp.sum(copies, axis=0)


def butterfly(x, axis):
    count = lax.axis_size(axis)
    bit = 1
    while bit < count:
        x = x + lax.ppermute(x, axis, [(i, i ^ bit) for i in range(count)])
        bit *= 2
    return x


def fit_kernel(shapes_ref, shapes_t_ref, video_ref, basis_ref, data_ref, mode_ref):
    step = pl.program_id(0)
    model = jnp.dot(shapes_ref[...], basis_ref[...], preferred_element_type=jnp.float32)
    resid = (model - video_ref[...].astype(jnp.float32)).astype(jnp.bfloat16)
    data_ref[...] = lax.dot_general(
        resid, basis_ref[...], (((1,), (1,)), ((), ())), preferred_element_type=jnp.float32
    )
    part = jnp.dot(shapes_t_ref[...], resid, preferred_element_type=jnp.float32)

    @pl.when(step == 0)
    def _():
        mode_ref[...] = part

    @pl.when(step > 0)
    def _():
        mode_ref[...] += part


def fit(shapes, video, valid, basis, tile=640):
    n_pixels, n_modes = shapes.shape
    n_frames = video.shape[1]
    flops = 3 * 2 * n_pixels * n_modes * n_frames
    moved = video.size * 2 + shapes.size * 4 + n_pixels * n_modes * 4 + n_modes * n_frames * 8
    return pl.pallas_call(
        fit_kernel,
        grid=(n_pixels // tile,),
        in_specs=[
            pl.BlockSpec((tile, n_modes), lambda i: (i, 0)),
            pl.BlockSpec((n_modes, tile), lambda i: (0, i)),
            pl.BlockSpec((tile, n_frames), lambda i: (i, 0)),
            pl.BlockSpec((n_modes, n_frames), lambda i: (0, 0)),
        ],
        out_specs=[
            pl.BlockSpec((tile, n_modes), lambda i: (i, 0)),
            pl.BlockSpec((n_modes, n_frames), lambda i: (0, 0)),
        ],
        out_shape=[
            jax.ShapeDtypeStruct((n_pixels, n_modes), jnp.float32),
            jax.ShapeDtypeStruct((n_modes, n_frames), jnp.float32),
        ],
        compiler_params=pltpu.CompilerParams(dimension_semantics=("arbitrary",)),
        cost_estimate=pl.CostEstimate(flops=flops, bytes_accessed=moved, transcendentals=0),
    )(shapes, (shapes * valid[:, None].astype(shapes.dtype)).T, video, basis)


def body(video, shapes, valid, omega, damping, phase):
    frames_local = video.shape[1]
    scale = FRAMES ** (-0.5)
    n_frm = lax.axis_size("frm")
    me = lax.axis_index("frm")
    first = me * frames_local
    times = (first + jnp.arange(frames_local)).astype(jnp.float32) / FRAMES
    envelope = jnp.exp(-(damping[:, None] * times[None, :]))
    angle_all = omega[:, None] * times[None, :] + phase[:, None]
    cosine_all = envelope * jnp.cos(angle_all)
    cosine, sine, basis = lax.optimization_barrier(
        (cosine_all, envelope * jnp.sin(angle_all), cosine_all.astype(jnp.bfloat16))
    )

    rows_local = shapes.shape[0] // IMG_W
    grid = shapes.reshape(rows_local, IMG_W, shapes.shape[1])
    padded = with_halo(grid, (("pix", 0),), 1).astype(jnp.float32)

    data_raw, mode_raw = fit(shapes, video, valid, basis)
    data_part = scale * data_raw * valid[:, None].astype(jnp.float32)
    local_terms = mode_terms(scale * mode_raw, cosine, sine, times)
    n_pixels, n_modes = data_part.shape
    quarter = n_pixels // n_frm
    parts = data_part.reshape(n_frm, quarter, n_modes)
    acc = jnp.take(parts, me, axis=0)
    for s in range(1, n_frm):
        send = jnp.take(parts, (me + s) % n_frm, axis=0).astype(jnp.bfloat16)
        got_part = lax.ppermute(send, "frm", [(i, (i + s) % n_frm) for i in range(n_frm)])
        acc = acc + got_part.astype(jnp.float32)
    terms = sum_over(local_terms, "pix")

    rows_total = rows_local * lax.axis_size("pix")
    rows_at = lax.axis_index("pix") * rows_local + jnp.arange(rows_local)
    count = ((rows_at > 0).astype(jnp.float32) + (rows_at < rows_total - 1).astype(jnp.float32))[
        :, None, None
    ]
    smooth = 4.0 * (count * grid.astype(jnp.float32) - padded[:-2] - padded[2:])
    smooth_parts = smooth.reshape(n_frm, quarter, n_modes)
    own = (acc + jnp.take(smooth_parts, me, axis=0)).astype(jnp.bfloat16)

    hi, lo = split_f32(terms)
    k = terms.shape[0]
    extra = (-(quarter + 2 * k)) % 16
    packet = jnp.concatenate([own, hi, lo, jnp.zeros((extra, n_modes), jnp.bfloat16)], axis=0)
    got = [packet]
    for s in range(1, n_frm):
        got.append(lax.ppermute(packet, "frm", [(i, (i + s) % n_frm) for i in range(n_frm)]))
    stacked = jnp.stack(got)
    ordered = jnp.take(stacked, (me - jnp.arange(n_frm)) % n_frm, axis=0)
    shape_grad = ordered[:, :quarter].reshape(n_pixels, n_modes)
    pieces = ordered[:, quarter : quarter + k].astype(jnp.float32) + ordered[
        :, quarter + k : quarter + 2 * k
    ].astype(jnp.float32)
    total = pieces[0]
    for f in range(1, n_frm):
        total = total + pieces[f]
    return (shape_grad, total[0], total[1], total[2])


def solution(mesh):
    placed = (P("pix", "frm"), P("pix", None), P("pix"), P(), P(), P())
    return jax.shard_map(
        body, mesh=mesh, in_specs=placed, out_specs=(P("pix", None), P(), P(), P()), check_vma=False
    )
```

```python
import jax
import jax.numpy as jnp
from jax import lax
from jax.experimental import pallas as pl
from jax.experimental.pallas import tpu as pltpu
from jax.sharding import PartitionSpec as P

FRAMES = 4096
IMG_W = 128


def with_halo(cells, sides, width):
    for axis, dim in sides:
        count = lax.axis_size(axis)
        ends = count - 1
        head = lax.slice_in_dim(cells, 0, width, axis=dim)
        tail = lax.slice_in_dim(cells, cells.shape[dim] - width, cells.shape[dim], axis=dim)
        cells = jnp.concatenate(
            [
                lax.ppermute(tail, axis, [(i, (i + 1) % count) for i in range(ends)]),
                cells,
                lax.ppermute(head, axis, [((i + 1) % count, i) for i in range(ends)]),
            ],
            axis=dim,
        )
    return cells


def mode_terms(basis_grad, cosine, sine, times):
    omega_part = jnp.sum(basis_grad * (-times[None, :] * sine), axis=1)
    damping_part = jnp.sum(basis_grad * (-times[None, :] * cosine), axis=1)
    phase_part = jnp.sum(basis_grad * -sine, axis=1)
    return jnp.stack([omega_part, damping_part, phase_part])


def split_f32(x):
    top = lax.reduce_precision(x, exponent_bits=8, mantissa_bits=7)
    return top.astype(jnp.bfloat16), (x - top).astype(jnp.bfloat16)


def sum_over(x, axis):
    count = lax.axis_size(axis)
    copies = lax.all_to_all(jnp.broadcast_to(x[None], (count,) + x.shape), axis, 0, 0, tiled=False)
    return jnp.sum(copies, axis=0)


def butterfly(x, axis):
    count = lax.axis_size(axis)
    bit = 1
    while bit < count:
        x = x + lax.ppermute(x, axis, [(i, i ^ bit) for i in range(count)])
        bit *= 2
    return x


def fit_kernel(shapes_ref, shapes_t_ref, video_ref, basis_ref, data_ref, mode_ref):
    step = pl.program_id(0)
    model = jnp.dot(shapes_ref[...], basis_ref[...], preferred_element_type=jnp.float32)
    resid = (model - video_ref[...].astype(jnp.float32)).astype(jnp.bfloat16)
    data_ref[...] = lax.dot_general(
        resid, basis_ref[...], (((1,), (1,)), ((), ())), preferred_element_type=jnp.float32
    )
    part = jnp.dot(shapes_t_ref[...], resid, preferred_element_type=jnp.float32)

    @pl.when(step == 0)
    def _():
        mode_ref[...] = part

    @pl.when(step > 0)
    def _():
        mode_ref[...] += part


def fit(shapes, video, valid, basis, tile=640):
    n_pixels, n_modes = shapes.shape
    n_frames = video.shape[1]
    flops = 3 * 2 * n_pixels * n_modes * n_frames
    moved = video.size * 2 + shapes.size * 4 + n_pixels * n_modes * 4 + n_modes * n_frames * 8
    return pl.pallas_call(
        fit_kernel,
        grid=(n_pixels // tile,),
        in_specs=[
            pl.BlockSpec((tile, n_modes), lambda i: (i, 0)),
            pl.BlockSpec((n_modes, tile), lambda i: (0, i)),
            pl.BlockSpec((tile, n_frames), lambda i: (i, 0)),
            pl.BlockSpec((n_modes, n_frames), lambda i: (0, 0)),
        ],
        out_specs=[
            pl.BlockSpec((tile, n_modes), lambda i: (i, 0)),
            pl.BlockSpec((n_modes, n_frames), lambda i: (0, 0)),
        ],
        out_shape=[
            jax.ShapeDtypeStruct((n_pixels, n_modes), jnp.float32),
            jax.ShapeDtypeStruct((n_modes, n_frames), jnp.float32),
        ],
        compiler_params=pltpu.CompilerParams(
            dimension_semantics=("arbitrary",), allow_input_fusion=[False, True, False, False]
        ),
        cost_estimate=pl.CostEstimate(flops=flops, bytes_accessed=moved, transcendentals=0),
    )(shapes, (shapes * valid[:, None].astype(shapes.dtype)).T, video, basis)


def body(video, shapes, valid, omega, damping, phase):
    frames_local = video.shape[1]
    scale = FRAMES ** (-0.5)
    n_frm = lax.axis_size("frm")
    me = lax.axis_index("frm")
    first = me * frames_local
    times = (first + jnp.arange(frames_local)).astype(jnp.float32) / FRAMES
    envelope = jnp.exp(-(damping[:, None] * times[None, :]))
    angle_all = omega[:, None] * times[None, :] + phase[:, None]
    cosine_all = envelope * jnp.cos(angle_all)
    cosine, sine, basis = lax.optimization_barrier(
        (cosine_all, envelope * jnp.sin(angle_all), cosine_all.astype(jnp.bfloat16))
    )

    rows_local = shapes.shape[0] // IMG_W
    grid = shapes.reshape(rows_local, IMG_W, shapes.shape[1])
    padded = with_halo(grid, (("pix", 0),), 1).astype(jnp.float32)

    data_raw, mode_raw = fit(shapes, video, valid, basis)
    data_part = scale * data_raw * valid[:, None].astype(jnp.float32)
    local_terms = mode_terms(scale * mode_raw, cosine, sine, times)
    n_pixels, n_modes = data_part.shape
    quarter = n_pixels // n_frm
    parts = data_part.reshape(n_frm, quarter, n_modes)
    acc = jnp.take(parts, me, axis=0)
    for s in range(1, n_frm):
        send = jnp.take(parts, (me + s) % n_frm, axis=0).astype(jnp.bfloat16)
        got_part = lax.ppermute(send, "frm", [(i, (i + s) % n_frm) for i in range(n_frm)])
        acc = acc + got_part.astype(jnp.float32)
    terms = sum_over(local_terms, "pix")

    rows_total = rows_local * lax.axis_size("pix")
    rows_at = lax.axis_index("pix") * rows_local + jnp.arange(rows_local)
    count = ((rows_at > 0).astype(jnp.float32) + (rows_at < rows_total - 1).astype(jnp.float32))[
        :, None, None
    ]
    smooth = 4.0 * (count * grid.astype(jnp.float32) - padded[:-2] - padded[2:])
    smooth_parts = smooth.reshape(n_frm, quarter, n_modes)
    own = (acc + jnp.take(smooth_parts, me, axis=0)).astype(jnp.bfloat16)

    hi, lo = split_f32(terms)
    k = terms.shape[0]
    extra = (-(quarter + 2 * k)) % 16
    packet = jnp.concatenate([own, hi, lo, jnp.zeros((extra, n_modes), jnp.bfloat16)], axis=0)
    got = [packet]
    for s in range(1, n_frm):
        got.append(lax.ppermute(packet, "frm", [(i, (i + s) % n_frm) for i in range(n_frm)]))
    stacked = jnp.stack(got)
    ordered = jnp.take(stacked, (me - jnp.arange(n_frm)) % n_frm, axis=0)
    shape_grad = ordered[:, :quarter].reshape(n_pixels, n_modes)
    pieces = ordered[:, quarter : quarter + k].astype(jnp.float32) + ordered[
        :, quarter + k : quarter + 2 * k
    ].astype(jnp.float32)
    total = pieces[0]
    for f in range(1, n_frm):
        total = total + pieces[f]
    return (shape_grad, total[0], total[1], total[2])


def solution(mesh):
    placed = (P("pix", "frm"), P("pix", None), P("pix"), P(), P(), P())
    return jax.shard_map(
        body, mesh=mesh, in_specs=placed, out_specs=(P("pix", None), P(), P(), P()), check_vma=False
    )
```

```python
import jax
import jax.numpy as jnp
from jax import lax
from jax.experimental import pallas as pl
from jax.experimental.pallas import tpu as pltpu
from jax.sharding import PartitionSpec as P

FRAMES = 4096
IMG_W = 128


def with_halo(cells, sides, width):
    for axis, dim in sides:
        count = lax.axis_size(axis)
        ends = count - 1
        head = lax.slice_in_dim(cells, 0, width, axis=dim)
        tail = lax.slice_in_dim(cells, cells.shape[dim] - width, cells.shape[dim], axis=dim)
        cells = jnp.concatenate(
            [
                lax.ppermute(tail, axis, [(i, (i + 1) % count) for i in range(ends)]),
                cells,
                lax.ppermute(head, axis, [((i + 1) % count, i) for i in range(ends)]),
            ],
            axis=dim,
        )
    return cells


def mode_terms(basis_grad, cosine, sine, times):
    omega_part = jnp.sum(basis_grad * (-times[None, :] * sine), axis=1)
    damping_part = jnp.sum(basis_grad * (-times[None, :] * cosine), axis=1)
    phase_part = jnp.sum(basis_grad * -sine, axis=1)
    return jnp.stack([omega_part, damping_part, phase_part])


def split_f32(x):
    top = lax.reduce_precision(x, exponent_bits=8, mantissa_bits=7)
    return top.astype(jnp.bfloat16), (x - top).astype(jnp.bfloat16)


def sum_over(x, axis):
    count = lax.axis_size(axis)
    copies = lax.all_to_all(jnp.broadcast_to(x[None], (count,) + x.shape), axis, 0, 0, tiled=False)
    return jnp.sum(copies, axis=0)


def butterfly(x, axis):
    count = lax.axis_size(axis)
    bit = 1
    while bit < count:
        x = x + lax.ppermute(x, axis, [(i, i ^ bit) for i in range(count)])
        bit *= 2
    return x


def fit_kernel(shapes_ref, shapes_t_ref, video_ref, basis_ref, data_ref, mode_ref):
    step = pl.program_id(0)
    model = jnp.dot(shapes_ref[...], basis_ref[...], preferred_element_type=jnp.float32)
    resid = (model - video_ref[...].astype(jnp.float32)).astype(jnp.bfloat16)
    data_ref[...] = lax.dot_general(
        resid, basis_ref[...], (((1,), (1,)), ((), ())), preferred_element_type=jnp.float32
    )
    part = jnp.dot(shapes_t_ref[...], resid, preferred_element_type=jnp.float32)

    @pl.when(step == 0)
    def _():
        mode_ref[...] = part

    @pl.when(step > 0)
    def _():
        mode_ref[...] += part


def fit(shapes, video, valid, basis, tile=640):
    n_pixels, n_modes = shapes.shape
    n_frames = video.shape[1]
    flops = 3 * 2 * n_pixels * n_modes * n_frames
    moved = video.size * 2 + shapes.size * 4 + n_pixels * n_modes * 4 + n_modes * n_frames * 8
    return pl.pallas_call(
        fit_kernel,
        grid=(n_pixels // tile,),
        in_specs=[
            pl.BlockSpec((tile, n_modes), lambda i: (i, 0)),
            pl.BlockSpec((n_modes, tile), lambda i: (0, i)),
            pl.BlockSpec((tile, n_frames), lambda i: (i, 0)),
            pl.BlockSpec((n_modes, n_frames), lambda i: (0, 0)),
        ],
        out_specs=[
            pl.BlockSpec((tile, n_modes), lambda i: (i, 0)),
            pl.BlockSpec((n_modes, n_frames), lambda i: (0, 0)),
        ],
        out_shape=[
            jax.ShapeDtypeStruct((n_pixels, n_modes), jnp.float32),
            jax.ShapeDtypeStruct((n_modes, n_frames), jnp.float32),
        ],
        compiler_params=pltpu.CompilerParams(
            dimension_semantics=("arbitrary",), allow_input_fusion=[False, True, False, True]
        ),
        cost_estimate=pl.CostEstimate(flops=flops, bytes_accessed=moved, transcendentals=0),
    )(shapes, (shapes * valid[:, None].astype(shapes.dtype)).T, video, basis)


def body(video, shapes, valid, omega, damping, phase):
    frames_local = video.shape[1]
    scale = FRAMES ** (-0.5)
    n_frm = lax.axis_size("frm")
    me = lax.axis_index("frm")
    first = me * frames_local
    times = (first + jnp.arange(frames_local)).astype(jnp.float32) / FRAMES
    envelope = jnp.exp(-(damping[:, None] * times[None, :]))
    angle_all = omega[:, None] * times[None, :] + phase[:, None]
    cosine_all = envelope * jnp.cos(angle_all)
    cosine, sine = lax.optimization_barrier((cosine_all, envelope * jnp.sin(angle_all)))
    basis = cosine.astype(jnp.bfloat16)

    rows_local = shapes.shape[0] // IMG_W
    grid = shapes.reshape(rows_local, IMG_W, shapes.shape[1])
    padded = with_halo(grid, (("pix", 0),), 1).astype(jnp.float32)

    data_raw, mode_raw = fit(shapes, video, valid, basis)
    data_part = scale * data_raw * valid[:, None].astype(jnp.float32)
    local_terms = mode_terms(scale * mode_raw, cosine, sine, times)
    n_pixels, n_modes = data_part.shape
    quarter = n_pixels // n_frm
    parts = data_part.reshape(n_frm, quarter, n_modes)
    acc = jnp.take(parts, me, axis=0)
    for s in range(1, n_frm):
        send = jnp.take(parts, (me + s) % n_frm, axis=0).astype(jnp.bfloat16)
        got_part = lax.ppermute(send, "frm", [(i, (i + s) % n_frm) for i in range(n_frm)])
        acc = acc + got_part.astype(jnp.float32)
    terms = sum_over(local_terms, "pix")

    rows_total = rows_local * lax.axis_size("pix")
    rows_at = lax.axis_index("pix") * rows_local + jnp.arange(rows_local)
    count = ((rows_at > 0).astype(jnp.float32) + (rows_at < rows_total - 1).astype(jnp.float32))[
        :, None, None
    ]
    smooth = 4.0 * (count * grid.astype(jnp.float32) - padded[:-2] - padded[2:])
    smooth_parts = smooth.reshape(n_frm, quarter, n_modes)
    own = (acc + jnp.take(smooth_parts, me, axis=0)).astype(jnp.bfloat16)

    hi, lo = split_f32(terms)
    k = terms.shape[0]
    extra = (-(quarter + 2 * k)) % 16
    packet = jnp.concatenate([own, hi, lo, jnp.zeros((extra, n_modes), jnp.bfloat16)], axis=0)
    got = [packet]
    for s in range(1, n_frm):
        got.append(lax.ppermute(packet, "frm", [(i, (i + s) % n_frm) for i in range(n_frm)]))
    stacked = jnp.stack(got)
    ordered = jnp.take(stacked, (me - jnp.arange(n_frm)) % n_frm, axis=0)
    shape_grad = ordered[:, :quarter].reshape(n_pixels, n_modes)
    pieces = ordered[:, quarter : quarter + k].astype(jnp.float32) + ordered[
        :, quarter + k : quarter + 2 * k
    ].astype(jnp.float32)
    total = pieces[0]
    for f in range(1, n_frm):
        total = total + pieces[f]
    return (shape_grad, total[0], total[1], total[2])


def solution(mesh):
    placed = (P("pix", "frm"), P("pix", None), P("pix"), P(), P(), P())
    return jax.shard_map(
        body, mesh=mesh, in_specs=placed, out_specs=(P("pix", None), P(), P(), P()), check_vma=False
    )
```
